256 devices in a mesh: view: 8 (over x_hi, y), slab: 32 (over x_lo, z, core).
Axes of the slice: x: 4 (x_hi: 2, x_lo: 2; x = x_hi * 2 + x_lo), y: 4, z: 8, core: 2. Of those that a mesh axis runs over, the one named last changes fastest.
Arguments:
- estimate: float32 [64, 128, 512], P('slab'), may hold values from 1 to 2
- view_data: float32 [8, 64, 128, 512], P('view', 'slab'), may hold values from 1.5 to 3.5
- background: float32 [8], replicated, may hold values from 0.2 to 0.8
- psf_xy: float32 [8, 8, 2, 17], replicated, may hold values from 0.05 to 1
- psf_z: float32 [8, 3], replicated, may hold values from 0.2 to 1
- view_order: int32 [8], replicated, may hold values from 0 to 7, as said below
- depth_index: int32 [64], P('slab'), may hold values from 0 to 7
Outputs:
- updated: float32 [8, 64, 128, 512], P('view', 'slab')
The draws below stay inside these ranges and needn't reach their ends.
Inputs may be any that keep to these rules, and one draw needn't show every extreme that they name: view_order[p] = (view_order[0] + p) mod 8: the views go once around in index order, starting from any view.
All inputs are finite; a program needn't handle non-finite values.
Results may differ from the reference program's by a relative error of at most 0.0001.
Values sent between devices are 32-bit elements; how exact they have to be, the bound alone decides.
No kernel may reach another device: no remote copies, remote signals or barrier semaphores. Data moves between devices by JAX's collectives and lax.ppermute only.
A program may use at most 128 MiB of HBM per device.

```python
import math
import jax
import jax.numpy as jnp
from jax import lax

Y = 128
X = 512
RZ = 1
ND = 8
KX = 17
KZ = 3
NV = 8
NZ = 64


def draw_view_order(key, part):
    start = jax.random.randint(jax.random.fold_in(key, 17), (), 0, NV, dtype=jnp.int32)
    return ((start + jnp.arange(NV, dtype=jnp.int32)) % NV).astype(jnp.int32)


def touch_ends(drawn, stream_key, least, high):
    dims = drawn.shape
    place = [jax.random.randint(jax.random.fold_in(stream_key, axis), (), 0, dims[axis]) for axis in range(len(dims))]
    drawn = drawn.at[tuple(place)].set(least)
    longest = dims.index(max(dims))
    place[longest] = (place[longest] + 1) % dims[longest]
    return drawn.at[tuple(place)].set(high)


def levels(rng, dims, shards, least, high):
    gain, own = 1.0, jax.random.fold_in(rng, 6)
    for dim, blocks in shards:
        draws = jnp.exp(jax.random.uniform(jax.random.fold_in(own, dim), (blocks,), jnp.float32, least / len(shards), high / len(shards)))
        gain = gain * jnp.repeat(draws, dims[dim] // blocks).reshape([-1 if axis == dim else 1 for axis in range(len(dims))])
    return gain


def setup_inputs(seed: int = 0) -> dict:
    key_list = jax.random.split(jax.random.key(seed), 8)
    return {
        "estimate": jnp.clip(1.0 + 1.0 * jax.random.uniform(key_list[0], (NZ, Y, X), jnp.float32) ** levels(key_list[0], (NZ, Y, X), ((0, 32),), -0.2, 0.2), 1.0, 2.0),
        "view_data": jnp.clip(1.5 + 2.0 * jax.random.uniform(key_list[1], (NV, NZ, Y, X), jnp.float32) ** levels(key_list[1], (NV, NZ, Y, X), ((0, 8), (1, 32)), -0.2, 0.2), 1.5, 3.5),
        "background": jnp.clip(jnp.exp(jax.random.uniform(key_list[2], (NV,), jnp.float32, math.log(0.2), math.log(0.8))), 0.2, 0.8),
        "psf_xy": jnp.clip(jnp.exp(jax.random.uniform(key_list[3], (NV, ND, 2, KX), jnp.float32, math.log(0.05), math.log(1.0))), 0.05, 1.0),
        "psf_z": jnp.clip(jnp.exp(jax.random.uniform(key_list[4], (NV, KZ), jnp.float32, math.log(0.2), math.log(1.0))), 0.2, 1.0),
        "view_order": draw_view_order(jax.random.fold_in(key_list[7], 71), 0),
        "depth_index": touch_ends(jax.random.randint(key_list[6], (NZ,), 0, ND), jax.random.fold_in(key_list[6], 1), 0, ND - 1).astype(jnp.int32),
    }


exact_mode = lax.Precision.HIGHEST


def tap_matrix(taps, block):
    count = taps.shape[-1]
    width = block + count - 1
    rows = jnp.arange(block, dtype=jnp.int32)[:, None]
    cols = jnp.arange(width, dtype=jnp.int32)[None, :]
    offset = cols - rows
    picks = (offset[:, :, None] == jnp.arange(count, dtype=jnp.int32)[None, None, :]).astype(taps.dtype)
    return jnp.einsum("st,abt->sab", taps, picks, precision=exact_mode)


def blur_rows(slices, taps):
    reach = (taps.shape[-1] - 1) // 2
    extent = slices.shape[1]
    block = min(128, extent)
    mats = tap_matrix(taps, block)
    padded = jnp.pad(slices, ((0, 0), (reach, reach), (0, 0)))
    windows = jnp.stack([padded[:, i * block : i * block + block + 2 * reach] for i in range(extent // block)], axis=1)
    out = jnp.einsum("sab,sibx->siax", mats, windows, precision=exact_mode)
    return out.reshape(slices.shape)


def blur_columns(slices, taps):
    reach = (taps.shape[-1] - 1) // 2
    extent = slices.shape[2]
    block = min(128, extent)
    mats = tap_matrix(taps, block)
    padded = jnp.pad(slices, ((0, 0), (0, 0), (reach, reach)))
    windows = jnp.stack([padded[:, :, i * block : i * block + block + 2 * reach] for i in range(extent // block)], axis=2)
    out = jnp.einsum("sab,syib->syia", mats, windows, precision=exact_mode)
    return out.reshape(slices.shape)


def xy_forward(slices, y_taps, x_taps):
    return blur_columns(blur_rows(slices, y_taps), x_taps)


def xy_adjoint(slices, y_taps, x_taps):
    return blur_columns(blur_rows(slices, y_taps[:, ::-1]), x_taps[:, ::-1])


def z_forward(padded, z_taps):
    reach = (z_taps.shape[0] - 1) // 2
    count = padded.shape[0] - 2 * reach
    total = z_taps[0] * padded[0:count]
    for step in range(1, z_taps.shape[0]):
        total = total + z_taps[step] * padded[step : step + count]
    return total


def z_adjoint(padded, z_taps):
    reach = (z_taps.shape[0] - 1) // 2
    count = padded.shape[0] - 2 * reach
    total = z_taps[0] * padded[2 * reach : 2 * reach + count]
    for step in range(1, z_taps.shape[0]):
        total = total + z_taps[step] * padded[2 * reach - step : 2 * reach - step + count]
    return total


def reference(estimate, view_data, background, psf_xy, psf_z, view_order, depth_index):
    xy_kernels = psf_xy / jnp.sum(psf_xy, axis=-1, keepdims=True)
    z_kernels = psf_z / jnp.sum(psf_z, axis=-1, keepdims=True)
    widths = ((RZ, RZ), (0, 0), (0, 0))
    current = estimate
    results = jnp.zeros(view_data.shape, jnp.float32)
    for position in range(NV):
        view_id = view_order[position]
        slice_taps = xy_kernels[view_id][depth_index]
        y_taps = slice_taps[:, 0]
        x_taps = slice_taps[:, 1]
        z_taps = z_kernels[view_id]
        blurred = xy_forward(z_forward(jnp.pad(current, widths), z_taps), y_taps, x_taps)
        quotient = view_data[view_id] / (blurred + background[view_id])
        correction = z_adjoint(jnp.pad(xy_adjoint(quotient, y_taps, x_taps), widths), z_taps)
        current = current * correction
        results = results.at[view_id].set(current)
    return results
```

```python
import jax
import jax.numpy as jnp
from jax import lax
from jax.sharding import PartitionSpec as P

exact_mode = lax.Precision.HIGHEST


def band_matrix(taps, n):
    count = taps.shape[-1]
    reach = (count - 1) // 2
    block = min(128, n)
    nblocks = n // block
    rows = lax.broadcasted_iota(jnp.int32, (block, block), 0)
    cols = lax.broadcasted_iota(jnp.int32, (block, block), 1)
    offsets = (-1, 0, 1) if nblocks > 1 else (0,)
    parts = {}
    for off in offsets:
        d = off * block + cols - rows + reach
        m = jnp.zeros(taps.shape[:1] + (block, block), taps.dtype)
        for t in range(count):
            m = m + jnp.where((d == t)[None], taps[:, t, None, None], 0.0)
        parts[off] = m
    if nblocks == 1:
        return parts[0]
    bi = lax.broadcasted_iota(jnp.int32, (nblocks, nblocks), 0)
    bj = lax.broadcasted_iota(jnp.int32, (nblocks, nblocks), 1)
    full = jnp.zeros(taps.shape[:1] + (nblocks, block, nblocks, block), taps.dtype)
    for off, m in parts.items():
        sel = (bj - bi == off)[None, :, None, :, None]
        full = full + jnp.where(sel, m[:, None, :, None, :], 0.0)
    return full.reshape(taps.shape[:1] + (n, n))


def halo(array, axis, width):
    size = lax.axis_size(axis)
    up = [(i, i + 1) for i in range(size - 1)]
    down = [(i + 1, i) for i in range(size - 1)]
    below = lax.ppermute(array[-width:], axis, up)
    above = lax.ppermute(array[:width], axis, down)
    return jnp.concatenate([below, array, above], axis=0)


def per_device(estimate, view_data, background, psf_xy, psf_z, view_order, depth_index):
    view_count = lax.axis_size("view")
    my_view = lax.axis_index("view")
    xy_kernels = psf_xy / jnp.sum(psf_xy, axis=-1, keepdims=True)
    z_kernels = psf_z / jnp.sum(psf_z, axis=-1, keepdims=True)
    data_all = lax.all_gather(view_data[0], "view", axis=0)
    count = estimate.shape[0]
    ny, nx = estimate.shape[1], estimate.shape[2]
    current = estimate
    results = jnp.zeros_like(estimate)
    for position in range(view_count):
        view_id = view_order[position]
        table = lax.dynamic_index_in_dim(xy_kernels, view_id, 0, keepdims=False)
        slice_taps = jnp.take(table, depth_index, axis=0)
        by = band_matrix(slice_taps[:, 0], ny)
        bx = band_matrix(slice_taps[:, 1], nx)
        kz = lax.dynamic_index_in_dim(z_kernels, view_id, 0, keepdims=False)
        offset = lax.dynamic_index_in_dim(background, view_id, 0, keepdims=False)
        data = lax.dynamic_index_in_dim(data_all, view_id, 0, keepdims=False)
        padded = halo(current, "slab", 1)
        c = kz[0] * padded[0:count]
        for k in range(1, 3):
            c = c + kz[k] * padded[k : k + count]
        t = jnp.einsum("lij,ljx->lix", by, c, precision=exact_mode)
        blurred = jnp.einsum("lix,lax->lia", t, bx, precision=exact_mode)
        quotient = data / (blurred + offset)
        u = jnp.einsum("lij,lix->ljx", by, quotient, precision=exact_mode)
        g = jnp.einsum("ljx,lxa->lja", u, bx, precision=exact_mode)
        gp = halo(g, "slab", 1)
        corr = kz[0] * gp[2 : 2 + count]
        for k in range(1, 3):
            corr = corr + kz[k] * gp[2 - k : 2 - k + count]
        current = current * corr
        results = jnp.where(my_view == view_id, current, results)
    return results[None]


def solution(mesh):
    return jax.shard_map(
        per_device,
        mesh=mesh,
        in_specs=(
            P("slab", None, None),
            P("view", "slab", None, None),
            P(),
            P(),
            P(),
            P(),
            P("slab"),
        ),
        out_specs=P("view", "slab", None, None),
        check_vma=False,
    )
```

```python
import jax
import jax.numpy as jnp
from jax import lax
from jax.sharding import PartitionSpec as P

RZ = 1


exact_mode = lax.Precision.HIGHEST


def padded_2(array, sides, width):
    for axis, dim in sides:
        size, length = (lax.axis_size(axis), array.shape[dim])
        up = [(i, (i + 1) % size) for i in range(size - 1)]
        down = [(j, i) for i, j in up]
        last = lax.slice_in_dim(array, length - width, length, axis=dim)
        initial = lax.slice_in_dim(array, 0, width, axis=dim)
        before = lax.ppermute(last, axis, up)
        after = lax.ppermute(initial, axis, down)
        array = jnp.concatenate([before, array, after], axis=dim)
    return array


def shifted(array, axis, by):
    size = lax.axis_size(axis)
    return lax.ppermute(array, axis, [(i, (i + by) % size) for i in range(size)])


def tap_matrix(taps, block):
    count = taps.shape[-1]
    width = block + count - 1
    rows = jnp.arange(block, dtype=jnp.int32)[:, None]
    cols = jnp.arange(width, dtype=jnp.int32)[None, :]
    offset = cols - rows
    picks = (offset[:, :, None] == jnp.arange(count, dtype=jnp.int32)[None, None, :]).astype(
        taps.dtype
    )
    return jnp.einsum("st,abt->sab", taps, picks, precision=exact_mode)


def blur_rows(slices, taps):
    reach = (taps.shape[-1] - 1) // 2
    extent = slices.shape[1]
    block = min(128, extent)
    mats = tap_matrix(taps, block)
    padded = jnp.pad(slices, ((0, 0), (reach, reach), (0, 0)))
    windows = jnp.stack([padded], axis=1)
    out = jnp.einsum("sab,sibx->siax", mats, windows, precision=exact_mode)
    return out.reshape(slices.shape)


def blur_columns(slices, taps):
    reach = (taps.shape[-1] - 1) // 2
    extent = slices.shape[2]
    block = min(128, extent)
    mats = tap_matrix(taps, block)
    padded = jnp.pad(slices, ((0, 0), (0, 0), (reach, reach)))
    windows = jnp.stack(
        [padded[:, :, i * block : i * block + block + 2 * reach] for i in range(extent // block)],
        axis=2,
    )
    out = jnp.einsum("sab,syib->syia", mats, windows, precision=exact_mode)
    return out.reshape(slices.shape)


def xy_forward(slices, y_taps, x_taps):
    return blur_columns(blur_rows(slices, y_taps), x_taps)


def xy_adjoint(slices, y_taps, x_taps):
    return blur_columns(blur_rows(slices, y_taps[:, ::-1]), x_taps[:, ::-1])


def z_forward(padded, z_taps):
    reach = (z_taps.shape[0] - 1) // 2
    count = padded.shape[0] - 2 * reach
    total = z_taps[0] * padded[0:count]
    for step in range(1, z_taps.shape[0]):
        total = total + z_taps[step] * padded[step : step + count]
    return total


def z_adjoint(padded, z_taps):
    reach = (z_taps.shape[0] - 1) // 2
    count = padded.shape[0] - 2 * reach
    total = z_taps[0] * padded[2 * reach : 2 * reach + count]
    for step in range(1, z_taps.shape[0]):
        total = total + z_taps[step] * padded[2 * reach - step : 2 * reach - step + count]
    return total


def per_device(estimate, view_data, background, psf_xy, psf_z, view_order, depth_index):
    view_count = lax.axis_size("view")
    my_view = lax.axis_index("view")
    levels = psf_xy.shape[1]
    kernel_len = psf_xy.shape[3]
    xy_kernels = psf_xy / jnp.sum(psf_xy, axis=-1, keepdims=True)
    z_kernels = psf_z / jnp.sum(psf_z, axis=-1, keepdims=True)
    level_hot = (depth_index[:, None] == jnp.arange(levels, dtype=jnp.int32)[None, :]).astype(
        jnp.float32
    )
    data_all = lax.all_gather(view_data[0], "view", axis=0)
    current = estimate
    results = jnp.zeros_like(estimate)
    for position in range(view_count):
        view_id = view_order[position]
        table = lax.dynamic_index_in_dim(xy_kernels, view_id, 0, keepdims=False).reshape(
            levels, 2 * kernel_len
        )
        slice_taps = jnp.dot(level_hot, table, precision=exact_mode).reshape(-1, 2, kernel_len)
        y_taps = slice_taps[:, 0]
        x_taps = slice_taps[:, 1]
        z_taps = lax.dynamic_index_in_dim(z_kernels, view_id, 0, keepdims=False)
        offset = lax.dynamic_index_in_dim(background, view_id, 0, keepdims=False)
        data = lax.dynamic_index_in_dim(data_all, view_id, 0, keepdims=False)
        padded = padded_2(current, (("slab", 0),), RZ)
        blurred = xy_forward(z_forward(padded, z_taps), y_taps, x_taps)
        quotient = data / (blurred + offset)
        back_field = padded_2(xy_adjoint(quotient, y_taps, x_taps), (("slab", 0),), RZ)
        correction = z_adjoint(back_field, z_taps)
        current = current * correction
        results = jnp.where(my_view == view_id, current, results)
    return results[None]


def solution(mesh):
    return jax.shard_map(
        per_device,
        mesh=mesh,
        in_specs=(
            P("slab", None, None),
            P("view", "slab", None, None),
            P(),
            P(),
            P(),
            P(),
            P("slab"),
        ),
        out_specs=P("view", "slab", None, None),
        check_vma=False,
    )
```

```python
import jax
import jax.numpy as jnp
from jax import lax
from jax.sharding import PartitionSpec as P

RZ = 1


exact_mode = lax.Precision.HIGHEST


def padded_2(array, sides, width):
    for axis, dim in sides:
        size, length = (lax.axis_size(axis), array.shape[dim])
        up = [(i, (i + 1) % size) for i in range(size - 1)]
        down = [(j, i) for i, j in up]
        last = lax.slice_in_dim(array, length - width, length, axis=dim)
        initial = lax.slice_in_dim(array, 0, width, axis=dim)
        before = lax.ppermute(last, axis, up)
        after = lax.ppermute(initial, axis, down)
        array = jnp.concatenate([before, array, after], axis=dim)
    return array


def shifted(array, axis, by):
    size = lax.axis_size(axis)
    return lax.ppermute(array, axis, [(i, (i + by) % size) for i in range(size)])


def tap_matrix(taps, block):
    count = taps.shape[-1]
    width = block + count - 1
    rows = jnp.arange(block, dtype=jnp.int32)[:, None]
    cols = jnp.arange(width, dtype=jnp.int32)[None, :]
    offset = cols - rows
    picks = (offset[:, :, None] == jnp.arange(count, dtype=jnp.int32)[None, None, :]).astype(
        taps.dtype
    )
    return jnp.einsum("st,abt->sab", taps, picks, precision=exact_mode)


def blur_rows(slices, taps):
    reach = (taps.shape[-1] - 1) // 2
    extent = slices.shape[1]
    block = min(128, extent)
    mats = tap_matrix(taps, block)
    padded = jnp.pad(slices, ((0, 0), (reach, reach), (0, 0)))
    windows = jnp.stack([padded], axis=1)
    out = jnp.einsum("sab,sibx->siax", mats, windows, precision=exact_mode)
    return out.reshape(slices.shape)


def blur_columns(slices, taps):
    reach = (taps.shape[-1] - 1) // 2
    extent = slices.shape[2]
    block = min(128, extent)
    mats = tap_matrix(taps, block)
    padded = jnp.pad(slices, ((0, 0), (0, 0), (reach, reach)))
    windows = jnp.stack(
        [padded[:, :, i * block : i * block + block + 2 * reach] for i in range(extent // block)],
        axis=2,
    )
    out = jnp.einsum("sab,syib->syia", mats, windows, precision=exact_mode)
    return out.reshape(slices.shape)


def xy_forward(slices, y_taps, x_taps):
    return blur_columns(blur_rows(slices, y_taps), x_taps)


def xy_adjoint(slices, y_taps, x_taps):
    return blur_columns(blur_rows(slices, y_taps[:, ::-1]), x_taps[:, ::-1])


def z_forward(padded, z_taps):
    reach = (z_taps.shape[0] - 1) // 2
    count = padded.shape[0] - 2 * reach
    total = z_taps[0] * padded[0:count]
    for step in range(1, z_taps.shape[0]):
        total = total + z_taps[step] * padded[step : step + count]
    return total


def z_adjoint(padded, z_taps):
    reach = (z_taps.shape[0] - 1) // 2
    count = padded.shape[0] - 2 * reach
    total = z_taps[0] * padded[2 * reach : 2 * reach + count]
    for step in range(1, z_taps.shape[0]):
        total = total + z_taps[step] * padded[2 * reach - step : 2 * reach - step + count]
    return total


def per_device(estimate, view_data, background, psf_xy, psf_z, view_order, depth_index):
    view_count = lax.axis_size("view")
    my_view = lax.axis_index("view")
    levels = psf_xy.shape[1]
    kernel_len = psf_xy.shape[3]
    xy_kernels = psf_xy / jnp.sum(psf_xy, axis=-1, keepdims=True)
    z_kernels = psf_z / jnp.sum(psf_z, axis=-1, keepdims=True)
    level_hot = (depth_index[:, None] == jnp.arange(levels, dtype=jnp.int32)[None, :]).astype(
        jnp.float32
    )
    local = view_data[0]
    received = [local]
    for by in range(1, view_count):
        received.append(shifted(local, "view", by))
    stacked = jnp.stack(received, axis=0)
    current = estimate
    results = jnp.zeros_like(estimate)
    for position in range(view_count):
        view_id = view_order[position]
        table = lax.dynamic_index_in_dim(xy_kernels, view_id, 0, keepdims=False).reshape(
            levels, 2 * kernel_len
        )
        slice_taps = jnp.dot(level_hot, table, precision=exact_mode).reshape(-1, 2, kernel_len)
        y_taps = slice_taps[:, 0]
        x_taps = slice_taps[:, 1]
        z_taps = lax.dynamic_index_in_dim(z_kernels, view_id, 0, keepdims=False)
        offset = lax.dynamic_index_in_dim(background, view_id, 0, keepdims=False)
        lag = (my_view - view_id) % view_count
        data = lax.dynamic_index_in_dim(stacked, lag, 0, keepdims=False)
        padded = padded_2(current, (("slab", 0),), RZ)
        blurred = xy_forward(z_forward(padded, z_taps), y_taps, x_taps)
        quotient = data / (blurred + offset)
        back_field = padded_2(xy_adjoint(quotient, y_taps, x_taps), (("slab", 0),), RZ)
        correction = z_adjoint(back_field, z_taps)
        current = current * correction
        results = jnp.where(my_view == view_id, current, results)
    return results[None]


def solution(mesh):
    return jax.shard_map(
        per_device,
        mesh=mesh,
        in_specs=(
            P("slab", None, None),
            P("view", "slab", None, None),
            P(),
            P(),
            P(),
            P(),
            P("slab"),
        ),
        out_specs=P("view", "slab", None, None),
        check_vma=False,
    )
```

```python
import jax
import jax.numpy as jnp
from jax import lax
from jax.sharding import PartitionSpec as P

RZ = 1


exact_mode = lax.Precision.HIGHEST


def halo(array, axis, width):
    size = lax.axis_size(axis)
    up = [(i, i + 1) for i in range(size - 1)]
    down = [(i + 1, i) for i in range(size - 1)]
    below = lax.ppermute(array[-width:], axis, up)
    above = lax.ppermute(array[:width], axis, down)
    return jnp.concatenate([below, array, above], axis=0)


def tap_matrix(taps, block):
    count = taps.shape[-1]
    width = block + count - 1
    rows = jnp.arange(block, dtype=jnp.int32)[:, None]
    cols = jnp.arange(width, dtype=jnp.int32)[None, :]
    offset = cols - rows
    picks = (offset[:, :, None] == jnp.arange(count, dtype=jnp.int32)[None, None, :]).astype(
        taps.dtype
    )
    return jnp.einsum("...t,abt->...ab", taps, picks, precision=exact_mode)


def band_matrix(taps, n):
    count = taps.shape[-1]
    reach = (count - 1) // 2
    block = min(128, n)
    mats = tap_matrix(taps, block)
    lead = taps.shape[:-1]
    rows = []
    for blk in range(n // block):
        start = blk * block - reach
        lo = max(start, 0)
        hi = min(start + block + 2 * reach, n)
        piece = mats[..., lo - start : hi - start]
        parts = []
        if lo > 0:
            parts.append(jnp.zeros(lead + (block, lo), taps.dtype))
        parts.append(piece)
        if hi < n:
            parts.append(jnp.zeros(lead + (block, n - hi), taps.dtype))
        rows.append(jnp.concatenate(parts, axis=-1))
    return jnp.concatenate(rows, axis=-2)


def per_device(estimate, view_data, background, psf_xy, psf_z, view_order, depth_index):
    view_count = lax.axis_size("view")
    my_view = lax.axis_index("view")
    xy_kernels = psf_xy / jnp.sum(psf_xy, axis=-1, keepdims=True)
    z_kernels = psf_z / jnp.sum(psf_z, axis=-1, keepdims=True)
    data_all = lax.all_gather(view_data[0], "view", axis=0)
    count, ny, nx = estimate.shape
    step_taps = jnp.take(jnp.take(xy_kernels, view_order, axis=0), depth_index, axis=1)
    by_all = band_matrix(step_taps[:, :, 0], ny)
    bx_all = band_matrix(step_taps[:, :, 1], nx)
    current = estimate
    results = jnp.zeros_like(estimate)
    for position in range(view_count):
        view_id = view_order[position]
        by = by_all[position]
        bx = bx_all[position]
        kz = lax.dynamic_index_in_dim(z_kernels, view_id, 0, keepdims=False)
        offset = lax.dynamic_index_in_dim(background, view_id, 0, keepdims=False)
        data = lax.dynamic_index_in_dim(data_all, view_id, 0, keepdims=False)
        padded = halo(current, "slab", RZ)
        c = kz[0] * padded[0:count]
        for k in range(1, 3):
            c = c + kz[k] * padded[k : k + count]
        t = jnp.einsum("lij,ljx->lix", by, c, precision=exact_mode)
        blurred = jnp.einsum("lix,lax->lia", t, bx, precision=exact_mode)
        quotient = data / (blurred + offset)
        u = jnp.einsum("lji,ljx->lix", by, quotient, precision=exact_mode)
        g = jnp.einsum("lix,lxa->lia", u, bx, precision=exact_mode)
        gp = halo(g, "slab", RZ)
        corr = kz[0] * gp[2 : 2 + count]
        for k in range(1, 3):
            corr = corr + kz[k] * gp[2 - k : 2 - k + count]
        current = current * corr
        results = jnp.where(my_view == view_id, current, results)
    return results[None]


def solution(mesh):
    return jax.shard_map(
        per_device,
        mesh=mesh,
        in_specs=(
            P("slab", None, None),
            P("view", "slab", None, None),
            P(),
            P(),
            P(),
            P(),
            P("slab"),
        ),
        out_specs=P("view", "slab", None, None),
        check_vma=False,
    )
```

```python
import jax
import jax.numpy as jnp
from jax import lax
from jax.sharding import PartitionSpec as P

RZ = 1


exact_mode = lax.Precision.HIGHEST


def padded_2(array, sides, width):
    for axis, dim in sides:
        size, length = (lax.axis_size(axis), array.shape[dim])
        up = [(i, (i + 1) % size) for i in range(size - 1)]
        down = [(j, i) for i, j in up]
        last = lax.slice_in_dim(array, length - width, length, axis=dim)
        initial = lax.slice_in_dim(array, 0, width, axis=dim)
        before = lax.ppermute(last, axis, up)
        after = lax.ppermute(initial, axis, down)
        array = jnp.concatenate([before, array, after], axis=dim)
    return array


def shifted(array, axis, by):
    size = lax.axis_size(axis)
    return lax.ppermute(array, axis, [(i, (i + by) % size) for i in range(size)])


def tap_matrix(taps, block):
    count = taps.shape[-1]
    width = block + count - 1
    rows = jnp.arange(block, dtype=jnp.int32)[:, None]
    cols = jnp.arange(width, dtype=jnp.int32)[None, :]
    offset = cols - rows
    picks = (offset[:, :, None] == jnp.arange(count, dtype=jnp.int32)[None, None, :]).astype(
        taps.dtype
    )
    return jnp.einsum("st,abt->sab", taps, picks, precision=exact_mode)


def blur_rows(slices, taps):
    reach = (taps.shape[-1] - 1) // 2
    extent = slices.shape[1]
    block = min(128, extent)
    mats = tap_matrix(taps, block)
    padded = jnp.pad(slices, ((0, 0), (reach, reach), (0, 0)))
    windows = jnp.stack([padded], axis=1)
    out = jnp.einsum("sab,sibx->siax", mats, windows, precision=exact_mode)
    return out.reshape(slices.shape)


def blur_columns(slices, taps):
    reach = (taps.shape[-1] - 1) // 2
    extent = slices.shape[2]
    block = min(128, extent)
    mats = tap_matrix(taps, block)
    padded = jnp.pad(slices, ((0, 0), (0, 0), (reach, reach)))
    windows = jnp.stack(
        [padded[:, :, i * block : i * block + block + 2 * reach] for i in range(extent // block)],
        axis=2,
    )
    out = jnp.einsum("sab,syib->syia", mats, windows, precision=exact_mode)
    return out.reshape(slices.shape)


def xy_forward(slices, y_taps, x_taps):
    return blur_columns(blur_rows(slices, y_taps), x_taps)


def xy_adjoint(slices, y_taps, x_taps):
    return blur_columns(blur_rows(slices, y_taps[:, ::-1]), x_taps[:, ::-1])


def z_forward(padded, z_taps):
    reach = (z_taps.shape[0] - 1) // 2
    count = padded.shape[0] - 2 * reach
    total = z_taps[0] * padded[0:count]
    for step in range(1, z_taps.shape[0]):
        total = total + z_taps[step] * padded[step : step + count]
    return total


def z_adjoint(padded, z_taps):
    reach = (z_taps.shape[0] - 1) // 2
    count = padded.shape[0] - 2 * reach
    total = z_taps[0] * padded[2 * reach : 2 * reach + count]
    for step in range(1, z_taps.shape[0]):
        total = total + z_taps[step] * padded[2 * reach - step : 2 * reach - step + count]
    return total


def per_device(estimate, view_data, background, psf_xy, psf_z, view_order, depth_index):
    view_count = lax.axis_size("view")
    my_view = lax.axis_index("view")
    levels = psf_xy.shape[1]
    kernel_len = psf_xy.shape[3]
    xy_kernels = psf_xy / jnp.sum(psf_xy, axis=-1, keepdims=True)
    z_kernels = psf_z / jnp.sum(psf_z, axis=-1, keepdims=True)
    level_hot = (depth_index[:, None] == jnp.arange(levels, dtype=jnp.int32)[None, :]).astype(
        jnp.float32
    )
    data_all = lax.all_gather(view_data[0], "view", axis=0)
    current = estimate
    padded = padded_2(current, (("slab", 0),), RZ)
    results = jnp.zeros_like(estimate)
    for position in range(view_count):
        view_id = view_order[position]
        table = lax.dynamic_index_in_dim(xy_kernels, view_id, 0, keepdims=False).reshape(
            levels, 2 * kernel_len
        )
        slice_taps = jnp.dot(level_hot, table, precision=exact_mode).reshape(-1, 2, kernel_len)
        y_taps = slice_taps[:, 0]
        x_taps = slice_taps[:, 1]
        z_taps = lax.dynamic_index_in_dim(z_kernels, view_id, 0, keepdims=False)
        offset = lax.dynamic_index_in_dim(background, view_id, 0, keepdims=False)
        data = lax.dynamic_index_in_dim(data_all, view_id, 0, keepdims=False)
        blurred = xy_forward(z_forward(padded, z_taps), y_taps, x_taps)
        quotient = data / (blurred + offset)
        back_field = padded_2(xy_adjoint(quotient, y_taps, x_taps), (("slab", 0),), 2 * RZ)
        padded = padded * z_adjoint(back_field, z_taps)
        current = padded[RZ:-RZ]
        results = jnp.where(my_view == view_id, current, results)
    return results[None]


def solution(mesh):
    return jax.shard_map(
        per_device,
        mesh=mesh,
        in_specs=(
            P("slab", None, None),
            P("view", "slab", None, None),
            P(),
            P(),
            P(),
            P(),
            P("slab"),
        ),
        out_specs=P("view", "slab", None, None),
        check_vma=False,
    )
```

```python
import jax
import jax.numpy as jnp
from jax import lax
from jax.sharding import PartitionSpec as P

RZ = 1


exact_mode = lax.Precision.HIGHEST
blur_mode = lax.Precision.HIGH


def padded_2(array, sides, width):
    for axis, dim in sides:
        size, length = (lax.axis_size(axis), array.shape[dim])
        up = [(i, (i + 1) % size) for i in range(size - 1)]
        down = [(j, i) for i, j in up]
        last = lax.slice_in_dim(array, length - width, length, axis=dim)
        initial = lax.slice_in_dim(array, 0, width, axis=dim)
        before = lax.ppermute(last, axis, up)
        after = lax.ppermute(initial, axis, down)
        array = jnp.concatenate([before, array, after], axis=dim)
    return array


def shifted(array, axis, by):
    size = lax.axis_size(axis)
    return lax.ppermute(array, axis, [(i, (i + by) % size) for i in range(size)])


def tap_matrix(taps, block):
    count = taps.shape[-1]
    width = block + count - 1
    rows = jnp.arange(block, dtype=jnp.int32)[:, None]
    cols = jnp.arange(width, dtype=jnp.int32)[None, :]
    offset = cols - rows
    picks = (offset[:, :, None] == jnp.arange(count, dtype=jnp.int32)[None, None, :]).astype(
        taps.dtype
    )
    return jnp.einsum("st,abt->sab", taps, picks, precision=exact_mode)


def blur_rows(slices, taps):
    reach = (taps.shape[-1] - 1) // 2
    extent = slices.shape[1]
    block = min(128, extent)
    mats = tap_matrix(taps, block)
    padded = jnp.pad(slices, ((0, 0), (reach, reach), (0, 0)))
    windows = jnp.stack([padded], axis=1)
    out = jnp.einsum("sab,sibx->siax", mats, windows, precision=blur_mode)
    return out.reshape(slices.shape)


def blur_columns(slices, taps):
    reach = (taps.shape[-1] - 1) // 2
    extent = slices.shape[2]
    block = min(128, extent)
    mats = tap_matrix(taps, block)
    padded = jnp.pad(slices, ((0, 0), (0, 0), (reach, reach)))
    windows = jnp.stack(
        [padded[:, :, i * block : i * block + block + 2 * reach] for i in range(extent // block)],
        axis=2,
    )
    out = jnp.einsum("sab,syib->syia", mats, windows, precision=blur_mode)
    return out.reshape(slices.shape)


def xy_forward(slices, y_taps, x_taps):
    return blur_columns(blur_rows(slices, y_taps), x_taps)


def xy_adjoint(slices, y_taps, x_taps):
    return blur_columns(blur_rows(slices, y_taps[:, ::-1]), x_taps[:, ::-1])


def z_forward(padded, z_taps):
    reach = (z_taps.shape[0] - 1) // 2
    count = padded.shape[0] - 2 * reach
    total = z_taps[0] * padded[0:count]
    for step in range(1, z_taps.shape[0]):
        total = total + z_taps[step] * padded[step : step + count]
    return total


def z_adjoint(padded, z_taps):
    reach = (z_taps.shape[0] - 1) // 2
    count = padded.shape[0] - 2 * reach
    total = z_taps[0] * padded[2 * reach : 2 * reach + count]
    for step in range(1, z_taps.shape[0]):
        total = total + z_taps[step] * padded[2 * reach - step : 2 * reach - step + count]
    return total


def per_device(estimate, view_data, background, psf_xy, psf_z, view_order, depth_index):
    view_count = lax.axis_size("view")
    my_view = lax.axis_index("view")
    levels = psf_xy.shape[1]
    kernel_len = psf_xy.shape[3]
    xy_kernels = psf_xy / jnp.sum(psf_xy, axis=-1, keepdims=True)
    z_kernels = psf_z / jnp.sum(psf_z, axis=-1, keepdims=True)
    level_hot = (depth_index[:, None] == jnp.arange(levels, dtype=jnp.int32)[None, :]).astype(
        jnp.float32
    )
    data_all = lax.all_gather(view_data[0], "view", axis=0)
    current = estimate
    padded = padded_2(current, (("slab", 0),), RZ)
    results = jnp.zeros_like(estimate)
    for position in range(view_count):
        view_id = view_order[position]
        table = lax.dynamic_index_in_dim(xy_kernels, view_id, 0, keepdims=False).reshape(
            levels, 2 * kernel_len
        )
        slice_taps = jnp.dot(level_hot, table, precision=exact_mode).reshape(-1, 2, kernel_len)
        y_taps = slice_taps[:, 0]
        x_taps = slice_taps[:, 1]
        z_taps = lax.dynamic_index_in_dim(z_kernels, view_id, 0, keepdims=False)
        offset = lax.dynamic_index_in_dim(background, view_id, 0, keepdims=False)
        data = lax.dynamic_index_in_dim(data_all, view_id, 0, keepdims=False)
        blurred = xy_forward(z_forward(padded, z_taps), y_taps, x_taps)
        quotient = data / (blurred + offset)
        back_field = padded_2(xy_adjoint(quotient, y_taps, x_taps), (("slab", 0),), 2 * RZ)
        padded = padded * z_adjoint(back_field, z_taps)
        current = padded[RZ:-RZ]
        results = jnp.where(my_view == view_id, current, results)
    return results[None]


def solution(mesh):
    return jax.shard_map(
        per_device,
        mesh=mesh,
        in_specs=(
            P("slab", None, None),
            P("view", "slab", None, None),
            P(),
            P(),
            P(),
            P(),
            P("slab"),
        ),
        out_specs=P("view", "slab", None, None),
        check_vma=False,
    )
```

```python
import jax
import jax.numpy as jnp
from jax import lax
from jax.sharding import PartitionSpec as P

RZ = 1


exact_mode = lax.Precision.HIGHEST
blur_mode = lax.Precision.HIGH


def halo(array, axis, width):
    size = lax.axis_size(axis)
    up = [(i, i + 1) for i in range(size - 1)]
    down = [(i + 1, i) for i in range(size - 1)]
    below = lax.ppermute(array[-width:], axis, up)
    above = lax.ppermute(array[:width], axis, down)
    return jnp.concatenate([below, array, above], axis=0)


def tap_matrix(taps, block):
    count = taps.shape[-1]
    width = block + count - 1
    rows = jnp.arange(block, dtype=jnp.int32)[:, None]
    cols = jnp.arange(width, dtype=jnp.int32)[None, :]
    offset = cols - rows
    picks = (offset[:, :, None] == jnp.arange(count, dtype=jnp.int32)[None, None, :]).astype(
        taps.dtype
    )
    return jnp.einsum("...t,abt->...ab", taps, picks, precision=exact_mode)


def band_matrix(mats, n, reach):
    block = mats.shape[-2]
    lead = mats.shape[:-2]
    rows = []
    for blk in range(n // block):
        start = blk * block - reach
        lo = max(start, 0)
        hi = min(start + block + 2 * reach, n)
        parts = []
        if lo > 0:
            parts.append(jnp.zeros(lead + (block, lo), mats.dtype))
        parts.append(mats[..., lo - start : hi - start])
        if hi < n:
            parts.append(jnp.zeros(lead + (block, n - hi), mats.dtype))
        rows.append(jnp.concatenate(parts, axis=-1))
    return jnp.concatenate(rows, axis=-2)


def per_device(estimate, view_data, background, psf_xy, psf_z, view_order, depth_index):
    view_count = lax.axis_size("view")
    my_view = lax.axis_index("view")
    levels = psf_xy.shape[1]
    kernel_len = psf_xy.shape[3]
    reach = (kernel_len - 1) // 2
    xy_kernels = psf_xy / jnp.sum(psf_xy, axis=-1, keepdims=True)
    z_kernels = psf_z / jnp.sum(psf_z, axis=-1, keepdims=True)
    data_all = lax.all_gather(view_data[0], "view", axis=0)
    count, ny, nx = estimate.shape
    views = psf_xy.shape[0]
    view_hot = (view_order[:, None] == jnp.arange(views, dtype=jnp.int32)[None, :]).astype(
        jnp.float32
    )
    level_hot = (depth_index[:, None] == jnp.arange(levels, dtype=jnp.int32)[None, :]).astype(
        jnp.float32
    )
    step_kernels = jnp.einsum("pv,vdk->pdk", view_hot, xy_kernels.reshape(views, levels, -1),
                              precision=exact_mode)
    step_taps = jnp.einsum("ld,pdk->plk", level_hot, step_kernels, precision=exact_mode)
    step_taps = step_taps.reshape(view_count, count, 2, kernel_len)
    mats_y = lax.optimization_barrier(tap_matrix(step_taps[:, :, 0], min(128, ny)))
    mats_x = lax.optimization_barrier(tap_matrix(step_taps[:, :, 1], min(128, nx)))
    by_all = band_matrix(mats_y, ny, reach)
    bx_all = band_matrix(mats_x, nx, reach)
    padded = halo(estimate, "slab", RZ)
    results = jnp.zeros_like(estimate)
    for position in range(view_count):
        view_id = view_order[position]
        by = by_all[position]
        bx = bx_all[position]
        kz = lax.dynamic_index_in_dim(z_kernels, view_id, 0, keepdims=False)
        offset = lax.dynamic_index_in_dim(background, view_id, 0, keepdims=False)
        data = lax.dynamic_index_in_dim(data_all, view_id, 0, keepdims=False)
        c = kz[0] * padded[0:count]
        for k in range(1, 3):
            c = c + kz[k] * padded[k : k + count]
        t = jnp.einsum("lij,ljx->lix", by, c, precision=blur_mode)
        blurred = jnp.einsum("lix,lax->lia", t, bx, precision=blur_mode)
        quotient = data / (blurred + offset)
        u = jnp.einsum("lji,ljx->lix", by, quotient, precision=blur_mode)
        g = jnp.einsum("lix,lxa->lia", u, bx, precision=blur_mode)
        gp = halo(g, "slab", 2 * RZ)
        corr = kz[0] * gp[2 : 2 + count + 2]
        for k in range(1, 3):
            corr = corr + kz[k] * gp[2 - k : 2 - k + count + 2]
        padded = padded * corr
        results = jnp.where(my_view == view_id, padded[RZ:-RZ], results)
    return results[None]


def solution(mesh):
    return jax.shard_map(
        per_device,
        mesh=mesh,
        in_specs=(
            P("slab", None, None),
            P("view", "slab", None, None),
            P(),
            P(),
            P(),
            P(),
            P("slab"),
        ),
        out_specs=P("view", "slab", None, None),
        check_vma=False,
    )
```

```python
import jax
import jax.numpy as jnp
from jax import lax
from jax.sharding import PartitionSpec as P

RZ = 1


exact_mode = lax.Precision.HIGHEST
blur_mode = lax.Precision.HIGH


def halo(array, axis, width):
    size = lax.axis_size(axis)
    up = [(i, i + 1) for i in range(size - 1)]
    down = [(i + 1, i) for i in range(size - 1)]
    below = lax.ppermute(array[-width:], axis, up)
    above = lax.ppermute(array[:width], axis, down)
    return jnp.concatenate([below, array, above], axis=0)


def tap_matrix(taps, block):
    count = taps.shape[-1]
    width = block + count - 1
    rows = jnp.arange(block, dtype=jnp.int32)[:, None]
    cols = jnp.arange(width, dtype=jnp.int32)[None, :]
    offset = cols - rows
    picks = (offset[:, :, None] == jnp.arange(count, dtype=jnp.int32)[None, None, :]).astype(
        taps.dtype
    )
    return jnp.einsum("...t,abt->...ab", taps, picks, precision=exact_mode)


def band_matrix(mats, n, reach):
    block = mats.shape[-2]
    nblocks = n // block
    diagonal = mats[..., reach : reach + block]
    if nblocks == 1:
        return diagonal
    zeros = jnp.zeros(mats.shape[:-1] + (block - reach,), mats.dtype)
    upper = jnp.concatenate([mats[..., block + reach :], zeros], axis=-1)
    lower = jnp.concatenate([zeros, mats[..., :reach]], axis=-1)
    empty = jnp.zeros_like(diagonal)
    pick = {0: diagonal, 1: upper, -1: lower}
    rows = [
        jnp.concatenate([pick.get(col - row, empty) for col in range(nblocks)], axis=-1)
        for row in range(nblocks)
    ]
    return jnp.concatenate(rows, axis=-2)


def per_device(estimate, view_data, background, psf_xy, psf_z, view_order, depth_index):
    view_count = lax.axis_size("view")
    my_view = lax.axis_index("view")
    levels = psf_xy.shape[1]
    kernel_len = psf_xy.shape[3]
    reach = (kernel_len - 1) // 2
    xy_kernels = psf_xy / jnp.sum(psf_xy, axis=-1, keepdims=True)
    z_kernels = psf_z / jnp.sum(psf_z, axis=-1, keepdims=True)
    data_all = lax.all_gather(view_data[0], "view", axis=0)
    count, ny, nx = estimate.shape
    views = psf_xy.shape[0]
    view_hot = (view_order[:, None] == jnp.arange(views, dtype=jnp.int32)[None, :]).astype(
        jnp.float32
    )
    level_hot = (depth_index[:, None] == jnp.arange(levels, dtype=jnp.int32)[None, :]).astype(
        jnp.float32
    )
    step_kernels = jnp.einsum("pv,vdk->pdk", view_hot, xy_kernels.reshape(views, levels, -1),
                              precision=exact_mode)
    step_taps = jnp.einsum("ld,pdk->plk", level_hot, step_kernels, precision=exact_mode)
    step_taps = step_taps.reshape(view_count, count, 2, kernel_len)
    taps_y = step_taps[:, :, 0]
    taps_x = step_taps[:, :, 1]
    mats = [
        lax.optimization_barrier(tap_matrix(taps, min(128, n)))
        for taps, n in ((taps_y, ny), (taps_y[..., ::-1], ny), (taps_x, nx), (taps_x[..., ::-1], nx))
    ]
    by_all = [band_matrix(mats[0][p], ny, reach) for p in range(view_count)]
    byr_all = [band_matrix(mats[1][p], ny, reach) for p in range(view_count)]
    bx_all = [band_matrix(mats[2][p], nx, reach) for p in range(view_count)]
    bxr_all = [band_matrix(mats[3][p], nx, reach) for p in range(view_count)]
    padded = halo(estimate, "slab", RZ)
    results = jnp.zeros_like(estimate)
    for position in range(view_count):
        view_id = view_order[position]
        by = by_all[position]
        kz = lax.dynamic_index_in_dim(z_kernels, view_id, 0, keepdims=False)
        offset = lax.dynamic_index_in_dim(background, view_id, 0, keepdims=False)
        data = lax.dynamic_index_in_dim(data_all, view_id, 0, keepdims=False)
        c = kz[0] * padded[0:count]
        for k in range(1, 3):
            c = c + kz[k] * padded[k : k + count]
        t = jnp.einsum("lij,ljx->lix", by, c, precision=blur_mode)
        blurred = jnp.einsum("lix,lax->lia", t, bx_all[position], precision=blur_mode)
        quotient = data / (blurred + offset)
        u = jnp.einsum("lij,ljx->lix", byr_all[position], quotient, precision=blur_mode)
        g = jnp.einsum("lix,lax->lia", u, bxr_all[position], precision=blur_mode)
        gp = halo(g, "slab", 2 * RZ)
        corr = kz[0] * gp[2 : 2 + count + 2]
        for k in range(1, 3):
            corr = corr + kz[k] * gp[2 - k : 2 - k + count + 2]
        padded = padded * corr
        results = jnp.where(my_view == view_id, padded[RZ:-RZ], results)
    return results[None]


def solution(mesh):
    return jax.shard_map(
        per_device,
        mesh=mesh,
        in_specs=(
            P("slab", None, None),
            P("view", "slab", None, None),
            P(),
            P(),
            P(),
            P(),
            P("slab"),
        ),
        out_specs=P("view", "slab", None, None),
        check_vma=False,
    )
```

```python
import jax
import jax.numpy as jnp
from jax import lax
from jax.sharding import PartitionSpec as P

RZ = 1


exact_mode = lax.Precision.HIGHEST
blur_mode = lax.Precision.HIGH


def halo(array, axis, width, pieces=2):
    size = lax.axis_size(axis)
    up = [(i, i + 1) for i in range(size - 1)]
    down = [(i + 1, i) for i in range(size - 1)]
    rows = array.shape[1]
    step = rows // pieces
    below, above = [], []
    for k in range(pieces):
        part = array[:, k * step : (k + 1) * step]
        below.append(lax.ppermute(part[-width:], axis, up))
        above.append(lax.ppermute(part[:width], axis, down))
    below = jnp.concatenate(below, axis=1)
    above = jnp.concatenate(above, axis=1)
    return jnp.concatenate([below, array, above], axis=0)


def tap_matrix(taps, block):
    count = taps.shape[-1]
    width = block + count - 1
    rows = jnp.arange(block, dtype=jnp.int32)[:, None]
    cols = jnp.arange(width, dtype=jnp.int32)[None, :]
    offset = cols - rows
    picks = (offset[:, :, None] == jnp.arange(count, dtype=jnp.int32)[None, None, :]).astype(
        taps.dtype
    )
    return jnp.einsum("...t,abt->...ab", taps, picks, precision=exact_mode)


def band_matrix(mats, n, reach):
    block = mats.shape[-2]
    nblocks = n // block
    diagonal = mats[..., reach : reach + block]
    if nblocks == 1:
        return diagonal
    zeros = jnp.zeros(mats.shape[:-1] + (block - reach,), mats.dtype)
    upper = jnp.concatenate([mats[..., block + reach :], zeros], axis=-1)
    lower = jnp.concatenate([zeros, mats[..., :reach]], axis=-1)
    empty = jnp.zeros_like(diagonal)
    pick = {0: diagonal, 1: upper, -1: lower}
    rows = [
        jnp.concatenate([pick.get(col - row, empty) for col in range(nblocks)], axis=-1)
        for row in range(nblocks)
    ]
    return jnp.concatenate(rows, axis=-2)


def per_device(estimate, view_data, background, psf_xy, psf_z, view_order, depth_index):
    view_count = lax.axis_size("view")
    my_view = lax.axis_index("view")
    levels = psf_xy.shape[1]
    kernel_len = psf_xy.shape[3]
    reach = (kernel_len - 1) // 2
    xy_kernels = psf_xy / jnp.sum(psf_xy, axis=-1, keepdims=True)
    z_kernels = psf_z / jnp.sum(psf_z, axis=-1, keepdims=True)
    data_all = lax.all_gather(view_data[0], "view", axis=0)
    count, ny, nx = estimate.shape
    views = psf_xy.shape[0]
    view_hot = (view_order[:, None] == jnp.arange(views, dtype=jnp.int32)[None, :]).astype(
        jnp.float32
    )
    level_hot = (depth_index[:, None] == jnp.arange(levels, dtype=jnp.int32)[None, :]).astype(
        jnp.float32
    )
    step_kernels = jnp.einsum("pv,vdk->pdk", view_hot, xy_kernels.reshape(views, levels, -1),
                              precision=exact_mode)
    step_taps = jnp.einsum("ld,pdk->plk", level_hot, step_kernels, precision=exact_mode)
    step_taps = step_taps.reshape(view_count, count, 2, kernel_len)
    taps_y = step_taps[:, :, 0]
    taps_x = step_taps[:, :, 1]
    mats = [
        lax.optimization_barrier(tap_matrix(taps, min(128, n)))
        for taps, n in ((taps_y, ny), (taps_y[..., ::-1], ny), (taps_x, nx), (taps_x[..., ::-1], nx))
    ]
    by_all = [band_matrix(mats[0][p], ny, reach) for p in range(view_count)]
    byr_all = [band_matrix(mats[1][p], ny, reach) for p in range(view_count)]
    bx_all = [band_matrix(mats[2][p], nx, reach) for p in range(view_count)]
    bxr_all = [band_matrix(mats[3][p], nx, reach) for p in range(view_count)]
    padded = halo(estimate, "slab", RZ)
    results = jnp.zeros_like(estimate)
    for position in range(view_count):
        view_id = view_order[position]
        by = by_all[position]
        kz = lax.dynamic_index_in_dim(z_kernels, view_id, 0, keepdims=False)
        offset = lax.dynamic_index_in_dim(background, view_id, 0, keepdims=False)
        data = lax.dynamic_index_in_dim(data_all, view_id, 0, keepdims=False)
        c = kz[0] * padded[0:count]
        for k in range(1, 3):
            c = c + kz[k] * padded[k : k + count]
        t = jnp.einsum("lij,ljx->lix", by, c, precision=blur_mode)
        blurred = jnp.einsum("lix,lax->lia", t, bx_all[position], precision=blur_mode)
        quotient = data / (blurred + offset)
        u = jnp.einsum("lij,ljx->lix", byr_all[position], quotient, precision=blur_mode)
        g = jnp.einsum("lix,lax->lia", u, bxr_all[position], precision=blur_mode)
        gp = halo(g, "slab", 2 * RZ)
        corr = kz[0] * gp[2 : 2 + count + 2]
        for k in range(1, 3):
            corr = corr + kz[k] * gp[2 - k : 2 - k + count + 2]
        padded = padded * corr
        results = jnp.where(my_view == view_id, padded[RZ:-RZ], results)
        padded, results = lax.optimization_barrier((padded, results))
    return results[None]


def solution(mesh):
    return jax.shard_map(
        per_device,
        mesh=mesh,
        in_specs=(
            P("slab", None, None),
            P("view", "slab", None, None),
            P(),
            P(),
            P(),
            P(),
            P("slab"),
        ),
        out_specs=P("view", "slab", None, None),
        check_vma=False,
    )
```

```python
import jax
import jax.numpy as jnp
from jax import lax
from jax.sharding import PartitionSpec as P

RZ = 1


exact_mode = lax.Precision.HIGHEST
blur_mode = lax.Precision.HIGH


def halo(array, axis, width):
    size = lax.axis_size(axis)
    up = [(i, i + 1) for i in range(size - 1)]
    down = [(i + 1, i) for i in range(size - 1)]
    below = lax.ppermute(array[-width:], axis, up)
    above = lax.ppermute(array[:width], axis, down)
    return jnp.concatenate([below, array, above], axis=0)


def tap_matrix(taps, block):
    count = taps.shape[-1]
    width = block + count - 1
    rows = jnp.arange(block, dtype=jnp.int32)[:, None]
    cols = jnp.arange(width, dtype=jnp.int32)[None, :]
    offset = cols - rows
    picks = (offset[:, :, None] == jnp.arange(count, dtype=jnp.int32)[None, None, :]).astype(
        taps.dtype
    )
    return jnp.einsum("...t,abt->...ab", taps, picks, precision=exact_mode)


def band_matrix(mats, n, reach):
    block = mats.shape[-2]
    nblocks = n // block
    diagonal = mats[..., reach : reach + block]
    if nblocks == 1:
        return diagonal
    zeros = jnp.zeros(mats.shape[:-1] + (block - reach,), mats.dtype)
    upper = jnp.concatenate([mats[..., block + reach :], zeros], axis=-1)
    lower = jnp.concatenate([zeros, mats[..., :reach]], axis=-1)
    empty = jnp.zeros_like(diagonal)
    pick = {0: diagonal, 1: upper, -1: lower}
    rows = [
        jnp.concatenate([pick.get(col - row, empty) for col in range(nblocks)], axis=-1)
        for row in range(nblocks)
    ]
    return jnp.concatenate(rows, axis=-2)


def per_device(estimate, view_data, background, psf_xy, psf_z, view_order, depth_index):
    view_count = lax.axis_size("view")
    my_view = lax.axis_index("view")
    levels = psf_xy.shape[1]
    kernel_len = psf_xy.shape[3]
    reach = (kernel_len - 1) // 2
    xy_kernels = psf_xy / jnp.sum(psf_xy, axis=-1, keepdims=True)
    z_kernels = psf_z / jnp.sum(psf_z, axis=-1, keepdims=True)
    local = view_data[0]
    received = [local]
    for by in range(1, lax.axis_size("view")):
        received.append(
            lax.ppermute(local, "view", [(i, (i + by) % view_count) for i in range(view_count)])
        )
    stacked = jnp.stack(received, axis=0)
    count, ny, nx = estimate.shape
    views = psf_xy.shape[0]
    view_hot = (view_order[:, None] == jnp.arange(views, dtype=jnp.int32)[None, :]).astype(
        jnp.float32
    )
    level_hot = (depth_index[:, None] == jnp.arange(levels, dtype=jnp.int32)[None, :]).astype(
        jnp.float32
    )
    step_kernels = jnp.einsum("pv,vdk->pdk", view_hot, xy_kernels.reshape(views, levels, -1),
                              precision=exact_mode)
    step_taps = jnp.einsum("ld,pdk->plk", level_hot, step_kernels, precision=exact_mode)
    step_taps = step_taps.reshape(view_count, count, 2, kernel_len)
    taps_y = step_taps[:, :, 0]
    taps_x = step_taps[:, :, 1]
    mats = [
        lax.optimization_barrier(tap_matrix(taps, min(128, n)))
        for taps, n in ((taps_y, ny), (taps_y[..., ::-1], ny), (taps_x, nx), (taps_x[..., ::-1], nx))
    ]
    by_all = [band_matrix(mats[0][p], ny, reach) for p in range(view_count)]
    byr_all = [band_matrix(mats[1][p], ny, reach) for p in range(view_count)]
    bx_all = [band_matrix(mats[2][p], nx, reach) for p in range(view_count)]
    bxr_all = [band_matrix(mats[3][p], nx, reach) for p in range(view_count)]
    padded = halo(estimate, "slab", RZ)
    results = jnp.zeros_like(estimate)
    for position in range(view_count):
        view_id = view_order[position]
        by = by_all[position]
        kz = lax.dynamic_index_in_dim(z_kernels, view_id, 0, keepdims=False)
        offset = lax.dynamic_index_in_dim(background, view_id, 0, keepdims=False)
        lag = (my_view - view_id) % view_count
        data = lax.dynamic_index_in_dim(stacked, lag, 0, keepdims=False)
        c = kz[0] * padded[0:count]
        for k in range(1, 3):
            c = c + kz[k] * padded[k : k + count]
        t = jnp.einsum("lij,ljx->lix", by, c, precision=blur_mode)
        blurred = jnp.einsum("lix,lax->lia", t, bx_all[position], precision=blur_mode)
        quotient = data / (blurred + offset)
        u = jnp.einsum("lij,ljx->lix", byr_all[position], quotient, precision=blur_mode)
        g = jnp.einsum("lix,lax->lia", u, bxr_all[position], precision=blur_mode)
        gp = halo(g, "slab", 2 * RZ)
        corr = kz[0] * gp[2 : 2 + count + 2]
        for k in range(1, 3):
            corr = corr + kz[k] * gp[2 - k : 2 - k + count + 2]
        padded = padded * corr
        results = jnp.where(my_view == view_id, padded[RZ:-RZ], results)
    return results[None]


def solution(mesh):
    return jax.shard_map(
        per_device,
        mesh=mesh,
        in_specs=(
            P("slab", None, None),
            P("view", "slab", None, None),
            P(),
            P(),
            P(),
            P(),
            P("slab"),
        ),
        out_specs=P("view", "slab", None, None),
        check_vma=False,
    )
```

```python
import jax
import jax.numpy as jnp
from jax import lax
from jax.sharding import PartitionSpec as P

RZ = 1


exact_mode = lax.Precision.HIGHEST
blur_mode = lax.Precision.HIGH


def halo(array, axis, width):
    size = lax.axis_size(axis)
    odd = lax.axis_index(axis) % 2 == 1
    top = array[-width:]
    bottom = array[:width]
    inner = [(i, i + 1) for i in range(0, size - 1, 2)] + [(i + 1, i) for i in range(0, size - 1, 2)]
    outer = [(i, i + 1) for i in range(1, size - 1, 2)] + [(i + 1, i) for i in range(1, size - 1, 2)]
    inner_got = lax.ppermute(jnp.where(odd, bottom, top), axis, inner)
    outer_got = lax.ppermute(jnp.where(odd, top, bottom), axis, outer)
    below = jnp.where(odd, inner_got, outer_got)
    above = jnp.where(odd, outer_got, inner_got)
    return jnp.concatenate([below, array, above], axis=0)


def tap_matrix(taps, block):
    count = taps.shape[-1]
    width = block + count - 1
    rows = jnp.arange(block, dtype=jnp.int32)[:, None]
    cols = jnp.arange(width, dtype=jnp.int32)[None, :]
    offset = cols - rows
    picks = (offset[:, :, None] == jnp.arange(count, dtype=jnp.int32)[None, None, :]).astype(
        taps.dtype
    )
    return jnp.einsum("...t,abt->...ab", taps, picks, precision=exact_mode)


def band_matrix(mats, n, reach):
    block = mats.shape[-2]
    nblocks = n // block
    diagonal = mats[..., reach : reach + block]
    if nblocks == 1:
        return diagonal
    zeros = jnp.zeros(mats.shape[:-1] + (block - reach,), mats.dtype)
    upper = jnp.concatenate([mats[..., block + reach :], zeros], axis=-1)
    lower = jnp.concatenate([zeros, mats[..., :reach]], axis=-1)
    empty = jnp.zeros_like(diagonal)
    pick = {0: diagonal, 1: upper, -1: lower}
    rows = [
        jnp.concatenate([pick.get(col - row, empty) for col in range(nblocks)], axis=-1)
        for row in range(nblocks)
    ]
    return jnp.concatenate(rows, axis=-2)


def per_device(estimate, view_data, background, psf_xy, psf_z, view_order, depth_index):
    view_count = lax.axis_size("view")
    my_view = lax.axis_index("view")
    levels = psf_xy.shape[1]
    kernel_len = psf_xy.shape[3]
    reach = (kernel_len - 1) // 2
    xy_kernels = psf_xy / jnp.sum(psf_xy, axis=-1, keepdims=True)
    z_kernels = psf_z / jnp.sum(psf_z, axis=-1, keepdims=True)
    data_all = lax.all_gather(view_data[0], "view", axis=0)
    count, ny, nx = estimate.shape
    views = psf_xy.shape[0]
    view_hot = (view_order[:, None] == jnp.arange(views, dtype=jnp.int32)[None, :]).astype(
        jnp.float32
    )
    level_hot = (depth_index[:, None] == jnp.arange(levels, dtype=jnp.int32)[None, :]).astype(
        jnp.float32
    )
    step_kernels = jnp.einsum("pv,vdk->pdk", view_hot, xy_kernels.reshape(views, levels, -1),
                              precision=exact_mode)
    step_taps = jnp.einsum("ld,pdk->plk", level_hot, step_kernels, precision=exact_mode)
    step_taps = step_taps.reshape(view_count, count, 2, kernel_len)
    taps_y = step_taps[:, :, 0]
    taps_x = step_taps[:, :, 1]
    mats = [
        lax.optimization_barrier(tap_matrix(taps, min(128, n)))
        for taps, n in ((taps_y, ny), (taps_y[..., ::-1], ny), (taps_x, nx), (taps_x[..., ::-1], nx))
    ]
    by_all = [band_matrix(mats[0][p], ny, reach) for p in range(view_count)]
    byr_all = [band_matrix(mats[1][p], ny, reach) for p in range(view_count)]
    bx_all = [band_matrix(mats[2][p], nx, reach) for p in range(view_count)]
    bxr_all = [band_matrix(mats[3][p], nx, reach) for p in range(view_count)]
    padded = halo(estimate, "slab", RZ)
    results = jnp.zeros_like(estimate)
    for position in range(view_count):
        view_id = view_order[position]
        by = by_all[position]
        kz = lax.dynamic_index_in_dim(z_kernels, view_id, 0, keepdims=False)
        offset = lax.dynamic_index_in_dim(background, view_id, 0, keepdims=False)
        data = lax.dynamic_index_in_dim(data_all, view_id, 0, keepdims=False)
        c = kz[0] * padded[0:count]
        for k in range(1, 3):
            c = c + kz[k] * padded[k : k + count]
        t = jnp.einsum("lij,ljx->lix", by, c, precision=blur_mode)
        blurred = jnp.einsum("lix,lax->lia", t, bx_all[position], precision=blur_mode)
        quotient = data / (blurred + offset)
        u = jnp.einsum("lij,ljx->lix", byr_all[position], quotient, precision=blur_mode)
        g = jnp.einsum("lix,lax->lia", u, bxr_all[position], precision=blur_mode)
        gp = halo(g, "slab", 2 * RZ)
        corr = kz[0] * gp[2 : 2 + count + 2]
        for k in range(1, 3):
            corr = corr + kz[k] * gp[2 - k : 2 - k + count + 2]
        padded = padded * corr
        results = jnp.where(my_view == view_id, padded[RZ:-RZ], results)
    return results[None]


def solution(mesh):
    return jax.shard_map(
        per_device,
        mesh=mesh,
        in_specs=(
            P("slab", None, None),
            P("view", "slab", None, None),
            P(),
            P(),
            P(),
            P(),
            P("slab"),
        ),
        out_specs=P("view", "slab", None, None),
        check_vma=False,
    )
```

```python
import jax
import jax.numpy as jnp
from jax import lax
from jax.sharding import PartitionSpec as P

RZ = 1


exact_mode = lax.Precision.HIGHEST
blur_mode = lax.Precision.HIGH


def halo(array, axis, width):
    size = lax.axis_size(axis)
    odd = lax.axis_index(axis) % 2 == 1
    top = array[-width:]
    bottom = array[:width]
    inner = [(i, i + 1) for i in range(0, size - 1, 2)] + [(i + 1, i) for i in range(0, size - 1, 2)]
    outer = [(i, i + 1) for i in range(1, size - 1, 2)] + [(i + 1, i) for i in range(1, size - 1, 2)]
    inner_got = lax.ppermute(jnp.where(odd, bottom, top), axis, inner)
    outer_got = lax.ppermute(jnp.where(odd, top, bottom), axis, outer)
    below = jnp.where(odd, inner_got, outer_got)
    above = jnp.where(odd, outer_got, inner_got)
    return jnp.concatenate([below, array, above], axis=0)


def tap_matrix(taps, block):
    count = taps.shape[-1]
    width = block + count - 1
    rows = jnp.arange(block, dtype=jnp.int32)[:, None]
    cols = jnp.arange(width, dtype=jnp.int32)[None, :]
    offset = cols - rows
    picks = (offset[:, :, None] == jnp.arange(count, dtype=jnp.int32)[None, None, :]).astype(
        taps.dtype
    )
    return jnp.einsum("...t,abt->...ab", taps, picks, precision=exact_mode)


def band_matrix(mats, n, reach):
    block = mats.shape[-2]
    nblocks = n // block
    diagonal = mats[..., reach : reach + block]
    if nblocks == 1:
        return diagonal
    zeros = jnp.zeros(mats.shape[:-1] + (block - reach,), mats.dtype)
    upper = jnp.concatenate([mats[..., block + reach :], zeros], axis=-1)
    lower = jnp.concatenate([zeros, mats[..., :reach]], axis=-1)
    empty = jnp.zeros_like(diagonal)
    pick = {0: diagonal, 1: upper, -1: lower}
    rows = [
        jnp.concatenate([pick.get(col - row, empty) for col in range(nblocks)], axis=-1)
        for row in range(nblocks)
    ]
    return jnp.concatenate(rows, axis=-2)


def per_device(estimate, view_data, background, psf_xy, psf_z, view_order, depth_index):
    view_count = lax.axis_size("view")
    my_view = lax.axis_index("view")
    levels = psf_xy.shape[1]
    kernel_len = psf_xy.shape[3]
    reach = (kernel_len - 1) // 2
    xy_kernels = psf_xy / jnp.sum(psf_xy, axis=-1, keepdims=True)
    z_kernels = psf_z / jnp.sum(psf_z, axis=-1, keepdims=True)
    data_all = lax.all_gather(view_data[0], "view", axis=0)
    count, ny, nx = estimate.shape
    views = psf_xy.shape[0]
    view_hot = (view_order[:, None] == jnp.arange(views, dtype=jnp.int32)[None, :]).astype(
        jnp.float32
    )
    level_hot = (depth_index[:, None] == jnp.arange(levels, dtype=jnp.int32)[None, :]).astype(
        jnp.float32
    )
    step_kernels = jnp.einsum("pv,vdk->pdk", view_hot, xy_kernels.reshape(views, levels, -1),
                              precision=exact_mode)
    step_taps = jnp.einsum("ld,pdk->plk", level_hot, step_kernels, precision=exact_mode)
    step_taps = step_taps.reshape(view_count, count, 2, kernel_len)
    taps_y = step_taps[:, :, 0]
    taps_x = step_taps[:, :, 1]
    mats = [
        lax.optimization_barrier(tap_matrix(taps, min(128, n)))
        for taps, n in ((taps_y, ny), (taps_y[..., ::-1], ny), (taps_x, nx), (taps_x[..., ::-1], nx))
    ]
    by_all = [band_matrix(mats[0][p], ny, reach) for p in range(view_count)]
    byr_all = [band_matrix(mats[1][p], ny, reach) for p in range(view_count)]
    bx_all = [band_matrix(mats[2][p], nx, reach) for p in range(view_count)]
    bxr_all = [band_matrix(mats[3][p], nx, reach) for p in range(view_count)]
    padded = halo(estimate, "slab", RZ)
    results = jnp.zeros_like(estimate)
    for position in range(view_count):
        view_id = view_order[position]
        by = by_all[position]
        kz = lax.dynamic_index_in_dim(z_kernels, view_id, 0, keepdims=False)
        offset = lax.dynamic_index_in_dim(background, view_id, 0, keepdims=False)
        data = lax.dynamic_index_in_dim(data_all, view_id, 0, keepdims=False)
        c = kz[0] * padded[0:count]
        for k in range(1, 3):
            c = c + kz[k] * padded[k : k + count]
        t = jnp.einsum("lij,ljx->lix", by, c, precision=blur_mode)
        blurred = jnp.einsum("lix,lax->lia", t, bx_all[position], precision=blur_mode)
        quotient = data / (blurred + offset)
        u = jnp.einsum("lij,ljx->lix", byr_all[position], quotient, precision=blur_mode)
        g = jnp.einsum("lix,lax->lia", u, bxr_all[position], precision=blur_mode)
        gp = halo(g, "slab", 2 * RZ)
        corr = kz[0] * gp[2 : 2 + count + 2]
        for k in range(1, 3):
            corr = corr + kz[k] * gp[2 - k : 2 - k + count + 2]
        padded = padded * corr
        results = jnp.where(my_view == view_id, padded[RZ:-RZ], results)
        padded, results = lax.optimization_barrier((padded, results))
    return results[None]


def solution(mesh):
    return jax.shard_map(
        per_device,
        mesh=mesh,
        in_specs=(
            P("slab", None, None),
            P("view", "slab", None, None),
            P(),
            P(),
            P(),
            P(),
            P("slab"),
        ),
        out_specs=P("view", "slab", None, None),
        check_vma=False,
    )
```

```python
import jax
import jax.numpy as jnp
from jax import lax
from jax.sharding import PartitionSpec as P

RZ = 1


exact_mode = lax.Precision.HIGHEST
blur_mode = lax.Precision.HIGH


def halo(array, axis, width):
    size = lax.axis_size(axis)
    odd = lax.axis_index(axis) % 2 == 1
    top = array[-width:]
    bottom = array[:width]
    inner = [(i, i + 1) for i in range(0, size - 1, 2)] + [(i + 1, i) for i in range(0, size - 1, 2)]
    outer = [(i, i + 1) for i in range(1, size - 1, 2)] + [(i + 1, i) for i in range(1, size - 1, 2)]
    inner_got = lax.ppermute(jnp.where(odd, bottom, top), axis, inner)
    outer_got = lax.ppermute(jnp.where(odd, top, bottom), axis, outer)
    below = jnp.where(odd, inner_got, outer_got)
    above = jnp.where(odd, outer_got, inner_got)
    return jnp.concatenate([below, array, above], axis=0)


def tap_matrix(taps, block):
    count = taps.shape[-1]
    width = block + count - 1
    rows = jnp.arange(block, dtype=jnp.int32)[:, None]
    cols = jnp.arange(width, dtype=jnp.int32)[None, :]
    offset = cols - rows
    picks = (offset[:, :, None] == jnp.arange(count, dtype=jnp.int32)[None, None, :]).astype(
        taps.dtype
    )
    return jnp.einsum("...t,abt->...ab", taps, picks, precision=exact_mode)


def band_matrix(mats, n, reach):
    block = mats.shape[-2]
    nblocks = n // block
    diagonal = mats[..., reach : reach + block]
    if nblocks == 1:
        return diagonal
    zeros = jnp.zeros(mats.shape[:-1] + (block - reach,), mats.dtype)
    upper = jnp.concatenate([mats[..., block + reach :], zeros], axis=-1)
    lower = jnp.concatenate([zeros, mats[..., :reach]], axis=-1)
    empty = jnp.zeros_like(diagonal)
    pick = {0: diagonal, 1: upper, -1: lower}
    rows = [
        jnp.concatenate([pick.get(col - row, empty) for col in range(nblocks)], axis=-1)
        for row in range(nblocks)
    ]
    return jnp.concatenate(rows, axis=-2)


def per_device(estimate, view_data, background, psf_xy, psf_z, view_order, depth_index):
    view_count = lax.axis_size("view")
    my_view = lax.axis_index("view")
    levels = psf_xy.shape[1]
    kernel_len = psf_xy.shape[3]
    reach = (kernel_len - 1) // 2
    xy_kernels = psf_xy / jnp.sum(psf_xy, axis=-1, keepdims=True)
    z_kernels = psf_z / jnp.sum(psf_z, axis=-1, keepdims=True)
    data_all = lax.all_gather(view_data[0], "view", axis=0)
    count, ny, nx = estimate.shape
    views = psf_xy.shape[0]
    view_hot = (view_order[:, None] == jnp.arange(views, dtype=jnp.int32)[None, :]).astype(
        jnp.float32
    )
    level_hot = (depth_index[:, None] == jnp.arange(levels, dtype=jnp.int32)[None, :]).astype(
        jnp.float32
    )
    step_kernels = jnp.einsum("pv,vdk->pdk", view_hot, xy_kernels.reshape(views, levels, -1),
                              precision=exact_mode)
    step_taps = jnp.einsum("ld,pdk->plk", level_hot, step_kernels, precision=exact_mode)
    step_taps = step_taps.reshape(view_count, count, 2, kernel_len)
    taps_y = step_taps[:, :, 0]
    taps_x = step_taps[:, :, 1]
    mats = [
        lax.optimization_barrier(tap_matrix(taps, min(128, n)))
        for taps, n in ((taps_y, ny), (taps_y[..., ::-1], ny), (taps_x, nx), (taps_x[..., ::-1], nx))
    ]
    by_all = [band_matrix(mats[0][p], ny, reach) for p in range(view_count)]
    byr_all = [band_matrix(mats[1][p], ny, reach) for p in range(view_count)]
    bx_all = [band_matrix(mats[2][p], nx, reach) for p in range(view_count)]
    bxr_all = [band_matrix(mats[3][p], nx, reach) for p in range(view_count)]
    padded = halo(estimate, "slab", RZ)
    results = jnp.zeros_like(estimate)
    for position in range(view_count):
        view_id = view_order[position]
        by = by_all[position]
        kz = lax.dynamic_index_in_dim(z_kernels, view_id, 0, keepdims=False)
        offset = lax.dynamic_index_in_dim(background, view_id, 0, keepdims=False)
        data = lax.dynamic_index_in_dim(data_all, view_id, 0, keepdims=False)
        c = kz[0] * padded[0:count]
        for k in range(1, 3):
            c = c + kz[k] * padded[k : k + count]
        c = lax.optimization_barrier(c)
        t = jnp.einsum("lij,ljx->lix", by, c, precision=blur_mode)
        blurred = jnp.einsum("lix,lax->lia", t, bx_all[position], precision=blur_mode)
        quotient = data / (blurred + offset)
        u = jnp.einsum("lij,ljx->lix", byr_all[position], quotient, precision=blur_mode)
        g = jnp.einsum("lix,lax->lia", u, bxr_all[position], precision=blur_mode)
        gp = halo(g, "slab", 2 * RZ)
        corr = kz[0] * gp[2 : 2 + count + 2]
        for k in range(1, 3):
            corr = corr + kz[k] * gp[2 - k : 2 - k + count + 2]
        padded = padded * corr
        results = jnp.where(my_view == view_id, padded[RZ:-RZ], results)
    return results[None]


def solution(mesh):
    return jax.shard_map(
        per_device,
        mesh=mesh,
        in_specs=(
            P("slab", None, None),
            P("view", "slab", None, None),
            P(),
            P(),
            P(),
            P(),
            P("slab"),
        ),
        out_specs=P("view", "slab", None, None),
        check_vma=False,
    )
```

```python
import jax
import jax.numpy as jnp
from jax import lax
from jax.sharding import PartitionSpec as P

RZ = 1


exact_mode = lax.Precision.HIGHEST
blur_mode = lax.Precision.HIGH


def halo(array, axis, width):
    size = lax.axis_size(axis)
    odd = lax.axis_index(axis) % 2 == 1
    top = array[-width:]
    bottom = array[:width]
    inner = [(i, i + 1) for i in range(0, size - 1, 2)] + [(i + 1, i) for i in range(0, size - 1, 2)]
    outer = [(i, i + 1) for i in range(1, size - 1, 2)] + [(i + 1, i) for i in range(1, size - 1, 2)]
    inner_got = lax.ppermute(jnp.where(odd, bottom, top), axis, inner)
    outer_got = lax.ppermute(jnp.where(odd, top, bottom), axis, outer)
    below = jnp.where(odd, inner_got, outer_got)
    above = jnp.where(odd, outer_got, inner_got)
    return jnp.concatenate([below, array, above], axis=0)


def tap_matrix(taps, block):
    count = taps.shape[-1]
    width = block + count - 1
    rows = jnp.arange(block, dtype=jnp.int32)[:, None]
    cols = jnp.arange(width, dtype=jnp.int32)[None, :]
    offset = cols - rows
    picks = (offset[:, :, None] == jnp.arange(count, dtype=jnp.int32)[None, None, :]).astype(
        taps.dtype
    )
    return jnp.einsum("...t,abt->...ab", taps, picks, precision=exact_mode)


def band_matrix(mats, n, reach):
    block = mats.shape[-2]
    nblocks = n // block
    diagonal = mats[..., reach : reach + block]
    if nblocks == 1:
        return diagonal
    zeros = jnp.zeros(mats.shape[:-1] + (block - reach,), mats.dtype)
    upper = jnp.concatenate([mats[..., block + reach :], zeros], axis=-1)
    lower = jnp.concatenate([zeros, mats[..., :reach]], axis=-1)
    empty = jnp.zeros_like(diagonal)
    pick = {0: diagonal, 1: upper, -1: lower}
    rows = [
        jnp.concatenate([pick.get(col - row, empty) for col in range(nblocks)], axis=-1)
        for row in range(nblocks)
    ]
    return jnp.concatenate(rows, axis=-2)


def per_device(estimate, view_data, background, psf_xy, psf_z, view_order, depth_index):
    view_count = lax.axis_size("view")
    my_view = lax.axis_index("view")
    levels = psf_xy.shape[1]
    kernel_len = psf_xy.shape[3]
    reach = (kernel_len - 1) // 2
    xy_kernels = psf_xy / jnp.sum(psf_xy, axis=-1, keepdims=True)
    z_kernels = psf_z / jnp.sum(psf_z, axis=-1, keepdims=True)
    data_all = lax.all_gather(view_data[0], "view", axis=0)
    count, ny, nx = estimate.shape
    views = psf_xy.shape[0]
    view_hot = (view_order[:, None] == jnp.arange(views, dtype=jnp.int32)[None, :]).astype(
        jnp.float32
    )
    level_hot = (depth_index[:, None] == jnp.arange(levels, dtype=jnp.int32)[None, :]).astype(
        jnp.float32
    )
    step_kernels = jnp.einsum("pv,vdk->pdk", view_hot, xy_kernels.reshape(views, levels, -1),
                              precision=exact_mode)
    step_taps = jnp.einsum("ld,pdk->plk", level_hot, step_kernels, precision=exact_mode)
    step_taps = step_taps.reshape(view_count, count, 2, kernel_len)
    taps_y = step_taps[:, :, 0]
    taps_x = step_taps[:, :, 1]
    mats = [
        lax.optimization_barrier(tap_matrix(taps, min(128, n)))
        for taps, n in ((taps_y, ny), (taps_y[..., ::-1], ny), (taps_x, nx), (taps_x[..., ::-1], nx))
    ]
    by_all = [band_matrix(mats[0][p], ny, reach) for p in range(view_count)]
    byr_all = [band_matrix(mats[1][p], ny, reach) for p in range(view_count)]
    bx_all = [band_matrix(mats[2][p], nx, reach) for p in range(view_count)]
    bxr_all = [band_matrix(mats[3][p], nx, reach) for p in range(view_count)]
    padded = halo(estimate, "slab", RZ)
    history = []
    for position in range(view_count):
        view_id = view_order[position]
        by = by_all[position]
        kz = lax.dynamic_index_in_dim(z_kernels, view_id, 0, keepdims=False)
        offset = lax.dynamic_index_in_dim(background, view_id, 0, keepdims=False)
        data = lax.dynamic_index_in_dim(data_all, view_id, 0, keepdims=False)
        c = kz[0] * padded[0:count]
        for k in range(1, 3):
            c = c + kz[k] * padded[k : k + count]
        t = jnp.einsum("lij,ljx->lix", by, c, precision=blur_mode)
        blurred = jnp.einsum("lix,lax->lia", t, bx_all[position], precision=blur_mode)
        quotient = data / (blurred + offset)
        u = jnp.einsum("lij,ljx->lix", byr_all[position], quotient, precision=blur_mode)
        g = jnp.einsum("lix,lax->lia", u, bxr_all[position], precision=blur_mode)
        gp = halo(g, "slab", 2 * RZ)
        corr = kz[0] * gp[2 : 2 + count + 2]
        for k in range(1, 3):
            corr = corr + kz[k] * gp[2 - k : 2 - k + count + 2]
        padded = padded * corr
        history.append(padded[RZ:-RZ])
    mine = (my_view - view_order[0]) % view_count
    return lax.dynamic_index_in_dim(jnp.stack(history, axis=0), mine, 0, keepdims=True)


def solution(mesh):
    return jax.shard_map(
        per_device,
        mesh=mesh,
        in_specs=(
            P("slab", None, None),
            P("view", "slab", None, None),
            P(),
            P(),
            P(),
            P(),
            P("slab"),
        ),
        out_specs=P("view", "slab", None, None),
        check_vma=False,
    )
```
